32 devices in a mesh: groups: 2 (over x), tm: 16 (over z, y, core).
Axes of the slice: x: 2, y: 2, z: 4, core: 2. Of those that a mesh axis runs over, the one named last changes fastest.
Arguments:
- feats: bfloat16 [32, 16, 32, 128], P(('groups', 'tm')), parts along dimension 0, may hold values from -6 to 6
- clip_lengths: int32 [8], P('groups'), parts along dimension 0, may hold values from 1 to 8, 16 in all
- reversed_clip: int32 [8], P('groups'), parts along dimension 0, may hold values 0 or 1
- merge_weight: bfloat16 [2, 3, 3, 256, 128], replicated, may hold values from -0.125 to 0.125
- block_weight: bfloat16 [2, 4, 3, 3, 128, 128], replicated, may hold values from -0.1875 to 0.1875
- out_weight: bfloat16 [256, 128], replicated, may hold values from -0.375 to 0.375
Outputs:
- merged: bfloat16 [32, 16, 32, 128], P(('groups', 'tm')), parts along dimension 0
The draws below stay inside these ranges and needn't reach their ends.
There are 2 independent parts, one for each index of `groups`. The reference program is written for one: setup_inputs(seed, part) draws one part's arguments, and reference() takes and returns one part's arrays. A program takes and returns all parts, laid end to end along the dimension named above; an argument that names none is the same for every part. Nothing has to cross between parts.
Inputs may be any that keep to these rules, and one draw needn't show every extreme that they name: `clip_lengths`: each clip holds 1 to 8 frames, the clips fill all 16 frames in order, one holds exactly 8.
All inputs are finite; a program needn't handle non-finite values.
Results may differ from the reference program's by a relative error of at most 0.018.
Values may be sent and summed in bfloat16 or wider, within the bound.
No kernel may reach another device: no remote copies, remote signals or barrier semaphores. Data moves between devices by JAX's collectives and lax.ppermute only.
A program may use at most 64 MiB of HBM per device.

```python
import math
import jax
import jax.numpy as jnp
import numpy as np
from jax import lax

C = 128
H = 16
W = 32
CLIP = 8
FRAMES = 16
NCL = 4


def with_ends(array, stream_key, low, top_value):
    extent = array.shape
    spot = [jax.random.randint(jax.random.fold_in(stream_key, axis), (), 0, extent[axis]) for axis in range(len(extent))]
    array = array.at[tuple(spot)].set(low)
    longest = extent.index(max(extent))
    spot[longest] = (spot[longest] + 1) % extent[longest]
    return array.at[tuple(spot)].set(top_value)


def shard_levels(key, dims, split, least, high):
    def one(axis_at, shards_of):
        heights = jax.random.uniform(jax.random.fold_in(jax.random.fold_in(key, 6), axis_at), (shards_of,), jnp.float32, least / len(split), high / len(split))
        return jnp.repeat(jnp.exp(heights), dims[axis_at] // shards_of).reshape((-1,) + (1,) * (len(dims) - axis_at - 1))

    level = one(*split[0])
    for cut in split[1:]:
        level = level * one(*cut)
    return level


def profile(count, total, reach, lean):
    portions = [(1 << 20) // math.isqrt(standing ** lean) + 1 for standing in range(2, count + 1)]
    rest, holding = total - reach - (count - 1), [1] * (count - 1)
    while rest > 0:
        candidates = [i for i in range(count - 1) if holding[i] < reach]
        pool, remaining = sum([portions[i] for i in candidates]), rest
        for i in candidates:
            addition = min(reach - holding[i], max(1, remaining * portions[i] // pool), rest)
            holding[i] = holding[i] + addition
            rest = rest - addition
    return np.array([reach] + holding)


def uneven_parts(stream_key, amount, total, most, lean):
    if amount == 2:
        one = jax.random.randint(stream_key, (), max(1, total - most), min(most, total - 1) + 1)
        return jnp.stack([one, total - one])
    lengths = jnp.asarray(profile(amount, total, most, lean), jnp.int32)
    couples = (amount - 1) // 2
    source_of, sink = lengths[1:1 + 2 * couples:2], lengths[2:2 + 2 * couples:2]
    margin = jnp.minimum(source_of - 1, most - sink)
    shifted = jax.random.randint(jax.random.fold_in(stream_key, 1), (couples,), 0, 1 << 20) % (margin + 1)
    lengths = lengths.at[1:1 + 2 * couples:2].set(source_of - shifted).at[2:2 + 2 * couples:2].set(sink + shifted)
    return lengths[jax.random.permutation(jax.random.fold_in(stream_key, 2), amount)]


def bell_draw(key, extent, spread, bound, split=(), kind=jnp.bfloat16):
    array = jax.random.normal(key, extent, jnp.float32) * spread
    if len(split) > 0:
        array = shard_levels(key, extent, split, -0.22, 0.18) * array
    return jnp.clip(array, min=-bound, max=bound).astype(kind)


def setup_inputs(seed: int = 0, part: int = 0) -> dict:
    keys = jax.random.split(jax.random.key(seed), 7)
    own_keys = jax.random.split(jax.random.fold_in(keys[6], part), 7)
    return {
        "feats": bell_draw(own_keys[0], (FRAMES, H, W, C), 1.0, 6.0, ((0, 16),)),
        "clip_lengths": uneven_parts(own_keys[1], NCL, FRAMES, CLIP, 0).astype(jnp.int32),
        "reversed_clip": with_ends((jax.random.randint(own_keys[2], (NCL,), 0, 2) < 1).astype(jnp.int32), jax.random.fold_in(own_keys[2], 1), 0, 1),
        "merge_weight": bell_draw(keys[3], (2, 3, 3, 2 * C, C), (18 * C) ** -0.5, 0.125),
        "block_weight": bell_draw(keys[4], (2, 4, 3, 3, C, C), (9 * C) ** -0.5, 0.1875),
        "out_weight": bell_draw(keys[5], (2 * C, C), (2 * C) ** -0.5, 0.375),
    }


def conv_tile(x, w):
    rows, cols, inner = x.shape
    padded = jnp.pad(x, ((1, 1), (1, 1), (0, 0)))
    pieces = []
    for i in range(3):
        for j in range(3):
            pieces.append(padded[i:i + rows, j:j + cols].reshape(rows * cols, inner))
    joined = jnp.concatenate(pieces, -1)
    acc = jnp.dot(joined, w.reshape(9 * inner, w.shape[-1]), preferred_element_type=jnp.float32)
    return acc.reshape(rows, cols, -1)


def recur_step(prev, feat, merge_w, block_w):
    y = conv_tile(jnp.concatenate([prev, feat], -1), merge_w)
    y = jnp.where(y > 0, y, 0.1 * y).astype(jnp.bfloat16)
    for blk in range(2):
        z = jnp.maximum(conv_tile(y, block_w[2 * blk]), 0.0).astype(jnp.bfloat16)
        y = (y.astype(jnp.float32) + conv_tile(z, block_w[2 * blk + 1])).astype(jnp.bfloat16)
    return y


def frame_flags(frame_ids, clip_lengths, reversed_clip):
    ends = jnp.cumsum(clip_lengths).astype(jnp.int32)
    starts = ends - clip_lengths
    is_start = jnp.any(frame_ids[:, None] == starts[None], 1)
    is_last = jnp.any(frame_ids[:, None] + 1 == ends[None], 1)
    clip_of = jnp.sum((ends[None] <= frame_ids[:, None]).astype(jnp.int32), 1)
    clip_ids = jnp.arange(clip_lengths.shape[0], dtype=jnp.int32)
    rev = jnp.sum(jnp.where(clip_ids[None] == clip_of[:, None], reversed_clip[None], 0), 1).astype(jnp.int32)
    return is_start, is_last, rev


def reference(feats, clip_lengths, reversed_clip, merge_weight, block_weight, out_weight):
    frames = feats.shape[0]
    frame_ids = jnp.arange(frames, dtype=jnp.int32)
    is_start, is_last, rev = frame_flags(frame_ids, clip_lengths, reversed_clip)
    zero = jnp.zeros(feats.shape[1:], jnp.bfloat16)

    def chain(flags, flip, reverse):
        def one(state, inputs):
            feat, reset, back = inputs
            prev = jnp.where(reset, zero, state)
            d = jnp.abs(back - flip).astype(jnp.int32)
            fw = lax.dynamic_index_in_dim(merge_weight, d, 0, keepdims=False)
            bw = lax.dynamic_index_in_dim(block_weight, d, 0, keepdims=False)
            out = recur_step(prev, feat, fw, bw)
            return out, out
        _, states = lax.scan(one, zero, (feats, flags, rev), reverse=reverse)
        return states

    chain_a = chain(is_start, 0, False)
    chain_b = chain(is_last, 1, True)
    sel = (rev > 0)[:, None, None, None]
    forward = jnp.where(sel, chain_b, chain_a)
    backward = jnp.where(sel, chain_a, chain_b)
    both = jnp.concatenate([forward, backward], -1).reshape(-1, out_weight.shape[0])
    merged = jnp.dot(both, out_weight, preferred_element_type=jnp.float32)
    return merged.reshape(feats.shape).astype(jnp.bfloat16)
```

```python
import jax
import jax.numpy as jnp
from jax import lax
from jax.sharding import PartitionSpec as P

CLIP = 8


def shifted(x, axis, by):
    devices = lax.axis_size(axis)
    pairs = [(i, i + by) for i in range(devices) if 0 <= i + by < devices]
    return lax.ppermute(x, axis, pairs)


def conv_tile(x, w):
    out = lax.conv_general_dilated(
        x[None], w, (1, 1), ((1, 1), (1, 1)),
        dimension_numbers=("NHWC", "HWIO", "NHWC"),
        preferred_element_type=jnp.float32,
    )
    return out[0]


def recur_step(prev, feat, merge_w, block_w):
    y = conv_tile(jnp.concatenate([prev, feat], -1), merge_w)
    y = jnp.where(y > 0, y, 0.1 * y).astype(jnp.bfloat16)
    for blk in range(2):
        z = jnp.maximum(conv_tile(y, block_w[2 * blk]), 0.0).astype(jnp.bfloat16)
        y = (y.astype(jnp.float32) + conv_tile(z, block_w[2 * blk + 1])).astype(jnp.bfloat16)
    return y


def frame_flags(frame_ids, clip_lengths, reversed_clip):
    ends = jnp.cumsum(clip_lengths)
    starts = ends - clip_lengths
    is_start = jnp.any(frame_ids[:, None] == starts[None], 1)
    is_last = jnp.any(frame_ids[:, None] + 1 == ends[None], 1)
    clip_of = jnp.sum((ends[None] <= frame_ids[:, None]).astype(jnp.int32), 1)
    clip_ids = jnp.arange(clip_lengths.shape[0], dtype=jnp.int32)
    rev = jnp.sum(jnp.where(clip_ids[None] == clip_of[:, None], reversed_clip[None], 0), 1)
    return (is_start, is_last, rev)


def on_device(feats, clip_lengths, reversed_clip, merge_weight, block_weight, out_weight):
    span = CLIP
    here = lax.axis_index("tm")
    feat = feats[0]
    zero = jnp.zeros(feat.shape, jnp.bfloat16)
    own_start, own_last, own_rev = frame_flags(jnp.reshape(here, (1,)), clip_lengths, reversed_clip)
    back = own_rev[0]
    merge_a = lax.dynamic_index_in_dim(merge_weight, back, 0, keepdims=False)
    block_a = lax.dynamic_index_in_dim(block_weight, back, 0, keepdims=False)
    merge_b = lax.dynamic_index_in_dim(merge_weight, 1 - back, 0, keepdims=False)
    block_b = lax.dynamic_index_in_dim(block_weight, 1 - back, 0, keepdims=False)

    def tick(_, carry):
        state_a, state_b = carry
        recv_a = shifted(state_a, "tm", 1)
        recv_b = shifted(state_b, "tm", -1)
        recv_a = jnp.where(own_start[0], zero, recv_a)
        recv_b = jnp.where(own_last[0], zero, recv_b)
        return (
            recur_step(recv_a, feat, merge_a, block_a),
            recur_step(recv_b, feat, merge_b, block_b),
        )

    chain_a, chain_b = lax.fori_loop(0, span, tick, (zero, zero))
    forward = jnp.where(back > 0, chain_b, chain_a)
    backward = jnp.where(back > 0, chain_a, chain_b)
    both = jnp.concatenate([forward, backward], -1).reshape(-1, out_weight.shape[0])
    merged = jnp.dot(both, out_weight, preferred_element_type=jnp.float32)
    return merged.reshape(feats.shape).astype(jnp.bfloat16)


def solution(mesh):
    return jax.shard_map(
        on_device,
        mesh=mesh,
        in_specs=(P(("groups", "tm"), None, None, None), P("groups"), P("groups"), P(), P(), P()),
        out_specs=P(("groups", "tm"), None, None, None),
        check_vma=False,
    )
```
